512 devices in a mesh: dp: 32 (over y, z_hi, core), loop: 16 (over x, z_lo).
Axes of the slice: x: 4, y: 8, z: 8 (z_hi: 2, z_lo: 4; z = z_hi * 4 + z_lo), core: 2. Of those that a mesh axis runs over, the one named last changes fastest.
Arguments:
- tokens: bfloat16 [4096, 2048], P('dp', 'loop'), may hold values from -6 to 6
- norm_gain: bfloat16 [2048], replicated, may hold values from 0.25 to 1.75
- route_ids: int32 [4096, 8], P('dp'), may hold values from 0 to 127, all different within a row; in each aligned block of 128 rows (0 to 127, 128 to 255, ...) at most 16 rows name the same one
- route_weights: float32 [4096, 8], P('dp'), may hold values from 0.1 to 1
- w_gate: bfloat16 [512, 384, 2048], P(('dp', 'loop')), may hold values from -0.125 to 0.125
- w_up: bfloat16 [512, 384, 2048], P(('dp', 'loop')), may hold values from -0.125 to 0.125
- w_down: bfloat16 [512, 384, 2048], P(('dp', 'loop')), may hold values from -0.15625 to 0.15625
Outputs:
- block_out: bfloat16 [4096, 2048], P('dp', 'loop')
The draws below stay inside these ranges and needn't reach their ends.
Inputs may be any that keep to these rules, and one draw needn't show every extreme that they name: `route_ids`: each row names 8 different experts. Within each aligned block of 128 rows no expert is named by more than 16 rows, and in some blocks an expert is named by exactly 16 rows.
All inputs are finite; a program needn't handle non-finite values.
Results may differ from the reference program's by a relative error of at most 0.0059.
Values may be sent and summed in bfloat16 or wider, within the bound.
No kernel may reach another device: no remote copies, remote signals or barrier semaphores. Data moves between devices by JAX's collectives and lax.ppermute only.
A program may use at most 64 MiB of HBM per device.

```python
import math
import jax
import jax.numpy as jnp
import numpy as np
from jax import lax

D = 2048
FF = 1536
EXPERTS = 128
TOP = 8
HGROUPS = 4
R = 128
CAP = 16
TOKENS = 4096
N_DP = 32


def steps_of(own_key, dims, split, low, top_value):
    def one(dim, blocks):
        steps = jax.random.uniform(jax.random.fold_in(jax.random.fold_in(own_key, 6), dim), (blocks,), jnp.float32, low / len(split), top_value / len(split))
        return jnp.repeat(jnp.exp(steps), dims[dim] // blocks).reshape((-1,) + (1,) * (len(dims) - dim - 1))

    level = one(*split[0])
    for cut in split[1:]:
        level = level * one(*cut)
    return level


def routed_block(stream_key, own, number, rows, amount, top, most, skew):
    ranking = jax.random.permutation(stream_key, amount)
    heavy_load, ordinary = portions_of(amount, rows * top, most, skew, True), portions_of(amount, rows * top, most, skew, False)
    places = jnp.arange(amount)

    def named(sizes, turn):
        used = int((sizes > 0).sum())
        fixed = max(1, used // 4)
        moved = fixed + (places - fixed + turn * (used - fixed)) % max(1, amount - fixed)
        return jnp.zeros((amount,), jnp.int32).at[ranking[jnp.where(places < fixed, places, moved)]].set(jnp.asarray(sizes, jnp.int32))

    sizes = jnp.where(number % 4 == 0, named(heavy_load, number // 4), named(ordinary, number - number // 4 - 1))
    mixed = jax.random.permutation(jax.random.fold_in(own, 3), amount)
    donor, taker = mixed[0:amount // 2 * 2:2], mixed[1:amount // 2 * 2:2]
    room = jnp.minimum(sizes[donor] - 1, most - sizes[taker]) // 2
    room = jnp.where((donor == ranking[0]) | (taker == ranking[0]) | (sizes[taker] == 0), 0, jnp.maximum(room, 0))
    moved = jax.random.randint(jax.random.fold_in(own, 4), (amount // 2,), 0, 1 << 20) % (room + 1)
    sizes = sizes.at[donor].add(-moved).at[taker].add(moved)
    labels = jnp.searchsorted(jnp.cumsum(sizes), jnp.arange(rows * top), side="right").astype(jnp.int32)
    listing = labels.reshape(top, rows).T
    listing = listing[jax.random.permutation(jax.random.fold_in(own, 1), rows)]
    turn = jax.random.randint(jax.random.fold_in(own, 2), (rows, 1), 0, top)
    return jnp.take_along_axis(listing, (jnp.arange(top)[None, :] + turn) % top, axis=1)


def portions_of(amount, total, bound, slope, full):
    loads = [(1 << 20) // math.isqrt(grade ** slope) + 1 for grade in range(1, amount + 1)]
    largest = bound if full else min(bound, max(-(-total // amount), total * loads[0] // sum(loads)))
    least = 1 if total - largest >= amount - 1 else 0
    given, spare = [largest] + [least] * (amount - 1), total - largest - least * (amount - 1)
    while spare > 0:
        movable = [i for i in range(1, amount) if given[i] < largest] or [i for i in range(1, amount) if given[i] < bound]
        whole, budget = sum([loads[i] for i in movable]), spare
        for i in movable:
            addition = min(bound - given[i], max(1, budget * loads[i] // whole), spare)
            given[i] = given[i] + addition
            spare = spare - addition
    return np.array(given)


def noise(own_key, dims, scale, bound, cuts=(), kind=jnp.bfloat16):
    values = scale * jax.random.normal(own_key, dims, jnp.float32)
    if cuts:
        values = values * steps_of(own_key, dims, cuts, -0.22, 0.18)
    return jnp.clip(values, -bound, bound).astype(kind)


def setup_inputs(seed: int = 0) -> dict:
    splits = jax.random.split(jax.random.key(seed), 8)
    tokens = noise(splits[0], (TOKENS, D), 1.0, 6.0, ((0, 32), (1, 16)))
    norm_gain = jnp.clip(1.0 + 0.15 * jax.random.normal(splits[1], (D,), jnp.float32), 0.25, 1.75).astype(jnp.bfloat16)
    route_ids_keys = jax.random.split(jax.random.fold_in(splits[2], 1), TOKENS // R)
    route_ids_turns = jax.random.permutation(jax.random.fold_in(splits[2], 3), TOKENS // R)
    route_ids = jax.vmap(lambda own, number: routed_block(jax.random.fold_in(splits[2], 2), own, number, R, EXPERTS, TOP, CAP, 2))(route_ids_keys, route_ids_turns).reshape((TOKENS, TOP))
    route_weights = jnp.clip(jnp.exp(math.log(1.0) - 2.3025851 * jax.random.uniform(splits[3], (TOKENS, TOP), jnp.float32) ** steps_of(splits[3], (TOKENS, TOP), ((0, 32),), -0.2, 0.2)), 0.1, 1.0)
    w_gate = noise(splits[4], (EXPERTS * HGROUPS, FF // HGROUPS, D), D ** -0.5, 0.125, ((0, 512),))
    w_up = noise(splits[5], (EXPERTS * HGROUPS, FF // HGROUPS, D), D ** -0.5, 0.125, ((0, 512),))
    w_down = noise(splits[6], (EXPERTS * HGROUPS, FF // HGROUPS, D), FF ** -0.5, 0.15625, ((0, 512),))
    return dict(tokens=tokens, norm_gain=norm_gain, route_ids=route_ids, route_weights=route_weights, w_gate=w_gate, w_up=w_up, w_down=w_down)


def reference(tokens, norm_gain, route_ids, route_weights, w_gate, w_up, w_down):
    values = tokens.astype(jnp.float32)
    row_scale = lax.rsqrt(lax.optimization_barrier(jnp.mean(values * values, axis=1, keepdims=True)) + 1e-06)
    normed = (values * row_scale * norm_gain.astype(jnp.float32)).astype(jnp.bfloat16)
    per_expert = N_DP * CAP
    flat_ids = route_ids.reshape(-1).astype(jnp.int32)
    onehot = (flat_ids[:, None] == jnp.arange(EXPERTS, dtype=jnp.int32)[None, :]).astype(jnp.int32)
    position = lax.optimization_barrier(jnp.sum((jnp.cumsum(onehot, axis=0) - onehot) * onehot, axis=1)).astype(jnp.int32)
    slot_index = flat_ids * per_expert + position
    pair_ids = jnp.arange(TOKENS * TOP, dtype=jnp.int32)
    slot_owner = jnp.full((EXPERTS * per_expert,), TOKENS, jnp.int32).at[slot_index].set(pair_ids // TOP)
    slot_weight = jnp.zeros((EXPERTS * per_expert,), jnp.float32).at[slot_index].set(route_weights.reshape(-1).astype(jnp.float32))
    slot_owner = slot_owner.reshape(EXPERTS, per_expert)
    slot_weight = slot_weight.reshape(EXPERTS, per_expert)
    padded = jnp.concatenate([normed, jnp.zeros((1, D), jnp.bfloat16)], axis=0)
    group_width = FF // HGROUPS

    def expert_step(total, item):
        gate_w, up_w, down_w, rows_idx, row_w = item
        batch = padded[rows_idx]
        gate_part = jnp.dot(batch, gate_w.T, preferred_element_type=jnp.float32)
        up_part = jnp.dot(batch, up_w.T, preferred_element_type=jnp.float32)
        hidden = (jax.nn.silu(gate_part) * up_part).astype(jnp.bfloat16)
        expert_parts = jnp.einsum('rsf,sfd->srd', hidden.reshape(per_expert, HGROUPS, group_width).astype(jnp.float32), down_w.reshape(HGROUPS, group_width, D).astype(jnp.float32), precision=lax.Precision.HIGHEST)
        rounded = lax.optimization_barrier(expert_parts.astype(jnp.bfloat16))
        contrib = lax.optimization_barrier(jnp.sum(rounded.astype(jnp.float32), axis=0)) * row_w[:, None]
        return (total.at[rows_idx].add(contrib), None)
    start = jnp.zeros((TOKENS + 1, D), jnp.float32)
    items = (w_gate.reshape(EXPERTS, FF, D), w_up.reshape(EXPERTS, FF, D), w_down.reshape(EXPERTS, FF, D), slot_owner, slot_weight)
    total, unused = lax.scan(expert_step, start, items)
    return (values + total[:TOKENS]).astype(jnp.bfloat16)
```

```python
import jax
import jax.numpy as jnp
from jax import lax
from jax.sharding import PartitionSpec as P

EXPERTS = 128
HGROUPS = 4
CAP = 16
EPS = 1e-06
BOTH = ("dp", "loop")


def slot_tables(route_ids):
    rows, top = route_ids.shape
    flat_ids = route_ids.reshape(-1)
    onehot = (flat_ids[:, None] == jnp.arange(EXPERTS, dtype=jnp.int32)[None, :]).astype(jnp.int32)
    position = jnp.sum((jnp.cumsum(onehot, axis=0) - onehot) * onehot, axis=1)
    return (flat_ids * CAP + position).reshape(rows, top)


def shards(tokens, norm_gain, route_ids, route_weights, w_gate, w_up, w_down):
    rows, width = tokens.shape
    top = route_ids.shape[1]
    groups = lax.axis_size("dp")
    loops = lax.axis_size("loop")
    pairs_here, hidden_width, full_width = w_gate.shape
    group_experts = EXPERTS // groups
    hgroups = loops // group_experts
    slots = slot_tables(route_ids)

    pick = (slots[:, :, None] == jnp.arange(EXPERTS * CAP, dtype=jnp.int32)[None, None, :])
    pick = jnp.any(pick, axis=1).astype(jnp.bfloat16)
    gathered = jnp.dot(pick.T, tokens, preferred_element_type=jnp.float32).astype(jnp.bfloat16)
    gathered = gathered.reshape(groups, group_experts, 1, CAP, width)
    send = jnp.broadcast_to(gathered, (groups, group_experts, hgroups, CAP, width))
    send = send.reshape(groups * loops * CAP, width)
    arrived = lax.all_to_all(send, BOTH, 0, 0, tiled=True)
    arrived = arrived.reshape(groups, loops, CAP, width).transpose(0, 2, 1, 3)
    arrived = arrived.reshape(groups * CAP, full_width)

    values = arrived.astype(jnp.float32)
    square_sum = jnp.sum(values * values, axis=1, keepdims=True)
    row_scale = lax.rsqrt(square_sum / full_width + EPS)
    normed = (values * row_scale * norm_gain.astype(jnp.float32)[None, :]).astype(jnp.bfloat16)

    gate_w = w_gate.reshape(pairs_here * hidden_width, full_width)
    up_w = w_up.reshape(pairs_here * hidden_width, full_width)
    down_w = w_down.reshape(pairs_here * hidden_width, full_width)
    gate = lax.dot_general(normed, gate_w, (((1,), (1,)), ((), ())), preferred_element_type=jnp.float32)
    up = lax.dot_general(normed, up_w, (((1,), (1,)), ((), ())), preferred_element_type=jnp.float32)
    hidden = (jax.nn.silu(gate) * up).astype(jnp.bfloat16)
    part = jnp.dot(hidden, down_w, preferred_element_type=jnp.float32).astype(jnp.bfloat16)

    back = part.reshape(groups, CAP, loops, width).transpose(0, 2, 1, 3)
    back = back.reshape(groups * loops * CAP, width)
    returned = lax.all_to_all(back, BOTH, 0, 0, tiled=True)
    returned = returned.reshape(groups, group_experts, hgroups, CAP, width).astype(jnp.float32)
    per_expert = jnp.sum(returned, axis=2).reshape(EXPERTS * CAP, width)

    picked = per_expert[slots.reshape(-1)].reshape(rows, top, width)
    mixed = jnp.sum(picked * route_weights[:, :, None], axis=1)
    return (tokens.astype(jnp.float32) + mixed).astype(jnp.bfloat16)


def solution(mesh):
    return jax.shard_map(
        shards,
        mesh=mesh,
        in_specs=(
            P("dp", "loop"),
            P(),
            P("dp", None),
            P("dp", None),
            P(BOTH, None, None),
            P(BOTH, None, None),
            P(BOTH, None, None),
        ),
        out_specs=P("dp", "loop"),
        check_vma=False,
    )
```

```python
import jax
import jax.numpy as jnp
from jax import lax
from jax.sharding import PartitionSpec as P

EXPERTS = 128
HGROUPS = 4
CAP = 16
EPS = 1e-06
BOTH = ("dp", "loop")


def slot_tables(route_ids):
    rows, top = route_ids.shape
    flat_ids = route_ids.reshape(-1)
    onehot = (flat_ids[:, None] == jnp.arange(EXPERTS, dtype=jnp.int32)[None, :]).astype(jnp.int32)
    position = jnp.sum((jnp.cumsum(onehot, axis=0) - onehot) * onehot, axis=1)
    return (flat_ids * CAP + position).reshape(rows, top)


def shards(tokens, norm_gain, route_ids, route_weights, w_gate, w_up, w_down):
    rows, width = tokens.shape
    top = route_ids.shape[1]
    groups = lax.axis_size("dp")
    loops = lax.axis_size("loop")
    pairs_here, hidden_width, full_width = w_gate.shape
    group_experts = EXPERTS // groups
    hgroups = loops // group_experts
    slots = slot_tables(route_ids)

    chosen = route_ids[:, :, None] == jnp.arange(EXPERTS, dtype=jnp.int32)[None, None, :]
    place = jnp.sum(jnp.where(chosen, (slots % CAP + 1)[:, :, None], 0), axis=1)
    pick = place[:, :, None] == jnp.arange(1, CAP + 1, dtype=jnp.int32)[None, None, :]
    pick = pick.reshape(rows, EXPERTS * CAP).astype(jnp.bfloat16)
    gathered = jnp.dot(pick.T, tokens, preferred_element_type=jnp.float32).astype(jnp.bfloat16)
    gathered = gathered.reshape(groups, group_experts, 1, CAP, width)
    send = jnp.broadcast_to(gathered, (groups, group_experts, hgroups, CAP, width))
    send = send.reshape(groups * loops * CAP, width)
    arrived = lax.all_to_all(send, BOTH, 0, 0, tiled=True)
    arrived = arrived.reshape(groups, loops, CAP, width)

    values = arrived.astype(jnp.float32)
    square_sum = jnp.sum(values * values, axis=(1, 3), keepdims=True)
    row_scale = lax.rsqrt(square_sum / full_width + EPS)
    gain = norm_gain.astype(jnp.float32).reshape(1, loops, 1, width)
    normed = (values * row_scale * gain).astype(jnp.bfloat16)

    gate_w = w_gate.reshape(pairs_here * hidden_width, loops, width)
    up_w = w_up.reshape(pairs_here * hidden_width, loops, width)
    down_w = w_down.reshape(pairs_here * hidden_width, loops, width)
    gate = jnp.einsum("dljf,ulf->dju", normed, gate_w, preferred_element_type=jnp.float32)
    up = jnp.einsum("dljf,ulf->dju", normed, up_w, preferred_element_type=jnp.float32)
    hidden = (jax.nn.silu(gate) * up).astype(jnp.bfloat16)
    part = jnp.einsum("dju,ulf->dljf", hidden, down_w, preferred_element_type=jnp.float32)
    part = part.astype(jnp.bfloat16)

    back = part.reshape(groups * loops * CAP, width)
    returned = lax.all_to_all(back, BOTH, 0, 0, tiled=True)
    returned = returned.reshape(groups, group_experts, hgroups, CAP, width).astype(jnp.float32)
    per_expert = jnp.sum(returned, axis=2).reshape(EXPERTS * CAP, width)

    picked = per_expert[slots.reshape(-1)].reshape(rows, top, width)
    mixed = jnp.sum(picked * route_weights[:, :, None], axis=1)
    return (tokens.astype(jnp.float32) + mixed).astype(jnp.bfloat16)


def solution(mesh):
    return jax.shard_map(
        shards,
        mesh=mesh,
        in_specs=(
            P("dp", "loop"),
            P(),
            P("dp", None),
            P("dp", None),
            P(BOTH, None, None),
            P(BOTH, None, None),
            P(BOTH, None, None),
        ),
        out_specs=P("dp", "loop"),
        check_vma=False,
    )
```

```python
import jax
import jax.numpy as jnp
from jax import lax
from jax.sharding import PartitionSpec as P

EXPERTS = 128
HGROUPS = 4
CAP = 16
EPS = 1e-06
BOTH = ("dp", "loop")


def slot_tables(route_ids):
    rows, top = route_ids.shape
    flat_ids = route_ids.reshape(-1)
    onehot = (flat_ids[:, None] == jnp.arange(EXPERTS, dtype=jnp.int32)[None, :]).astype(jnp.int32)
    position = jnp.sum((jnp.cumsum(onehot, axis=0) - onehot) * onehot, axis=1)
    return (flat_ids * CAP + position).reshape(rows, top)


def shards(tokens, norm_gain, route_ids, route_weights, w_gate, w_up, w_down):
    rows, width = tokens.shape
    top = route_ids.shape[1]
    groups = lax.axis_size("dp")
    loops = lax.axis_size("loop")
    pairs_here, hidden_width, full_width = w_gate.shape
    group_experts = EXPERTS // groups
    hgroups = loops // group_experts
    slots = slot_tables(route_ids)

    chosen = route_ids[:, :, None] == jnp.arange(EXPERTS, dtype=jnp.int32)[None, None, :]
    place = jnp.sum(jnp.where(chosen, (slots % CAP + 1)[:, :, None], 0), axis=1)
    pick3 = place[:, :, None] == jnp.arange(1, CAP + 1, dtype=jnp.int32)[None, None, :]
    pick = pick3.reshape(rows, EXPERTS * CAP).astype(jnp.bfloat16)
    gathered = jnp.dot(pick.T, tokens, preferred_element_type=jnp.float32).astype(jnp.bfloat16)
    gathered = gathered.reshape(groups, group_experts, 1, CAP, width)
    send = jnp.broadcast_to(gathered, (groups, group_experts, hgroups, CAP, width))
    send = send.reshape(groups * loops * CAP, width)
    arrived = lax.all_to_all(send, BOTH, 0, 0, tiled=True)
    arrived = arrived.reshape(groups, loops, CAP, width)

    values = arrived.astype(jnp.float32)
    square_sum = jnp.sum(values * values, axis=(1, 3), keepdims=True)
    row_scale = lax.rsqrt(square_sum / full_width + EPS)
    gain = norm_gain.astype(jnp.float32).reshape(1, loops, 1, width)
    normed = lax.optimization_barrier((values * row_scale * gain).astype(jnp.bfloat16))

    gate_w = w_gate.reshape(pairs_here * hidden_width, loops, width)
    up_w = w_up.reshape(pairs_here * hidden_width, loops, width)
    down_w = w_down.reshape(pairs_here * hidden_width, loops, width)
    gate = jnp.einsum("dljf,ulf->dju", normed, gate_w, preferred_element_type=jnp.float32)
    up = jnp.einsum("dljf,ulf->dju", normed, up_w, preferred_element_type=jnp.float32)
    hidden = lax.optimization_barrier((jax.nn.silu(gate) * up).astype(jnp.bfloat16))
    part = jnp.einsum("dju,ulf->dljf", hidden, down_w, preferred_element_type=jnp.float32)
    part = part.astype(jnp.bfloat16)

    back = part.reshape(groups * loops * CAP, width)
    returned = lax.all_to_all(back, BOTH, 0, 0, tiled=True)
    returned = returned.reshape(groups, group_experts, hgroups, CAP, width).astype(jnp.float32)
    per_expert = jnp.sum(returned, axis=2).reshape(EXPERTS * CAP, width)

    weight_of = jnp.sum(jnp.where(chosen, route_weights[:, :, None], 0.0), axis=1)
    combine = jnp.where(pick3, weight_of[:, :, None], 0.0).reshape(rows, EXPERTS * CAP)
    mixed = jnp.dot(combine, per_expert, precision=lax.Precision.HIGHEST, preferred_element_type=jnp.float32)
    return (tokens.astype(jnp.float32) + mixed).astype(jnp.bfloat16)


def solution(mesh):
    return jax.shard_map(
        shards,
        mesh=mesh,
        in_specs=(
            P("dp", "loop"),
            P(),
            P("dp", None),
            P("dp", None),
            P(BOTH, None, None),
            P(BOTH, None, None),
            P(BOTH, None, None),
        ),
        out_specs=P("dp", "loop"),
        check_vma=False,
    )
```

```python
import jax
import jax.numpy as jnp
from jax import lax
from jax.sharding import PartitionSpec as P

EXPERTS = 128
HGROUPS = 4
CAP = 16
EPS = 1e-06
BOTH = ("dp", "loop")


def slot_tables(route_ids):
    rows, top = route_ids.shape
    flat_ids = route_ids.reshape(-1)
    onehot = (flat_ids[:, None] == jnp.arange(EXPERTS, dtype=jnp.int32)[None, :]).astype(jnp.int32)
    position = jnp.sum((jnp.cumsum(onehot, axis=0) - onehot) * onehot, axis=1)
    return (flat_ids * CAP + position).reshape(rows, top)


def shards(tokens, norm_gain, route_ids, route_weights, w_gate, w_up, w_down):
    rows, width = tokens.shape
    top = route_ids.shape[1]
    groups = lax.axis_size("dp")
    loops = lax.axis_size("loop")
    pairs_here, hidden_width, full_width = w_gate.shape
    group_experts = EXPERTS // groups
    hgroups = loops // group_experts
    slots = slot_tables(route_ids)

    chosen = route_ids[:, :, None] == jnp.arange(EXPERTS, dtype=jnp.int32)[None, None, :]
    place = jnp.sum(jnp.where(chosen, (slots % CAP + 1)[:, :, None], 0), axis=1)
    pick3 = place[:, :, None] == jnp.arange(1, CAP + 1, dtype=jnp.int32)[None, None, :]
    pick4 = jnp.broadcast_to(
        pick3.reshape(rows, groups, group_experts, 1, CAP),
        (rows, groups, group_experts, hgroups, CAP),
    ).reshape(rows, groups * loops * CAP).astype(jnp.bfloat16)
    send = jnp.dot(pick4.T, tokens, preferred_element_type=jnp.float32).astype(jnp.bfloat16)
    arrived = lax.all_to_all(send, BOTH, 0, 0, tiled=True)
    arrived = arrived.reshape(groups, loops, CAP, width)

    values = arrived.astype(jnp.float32)
    square_sum = jnp.sum(values * values, axis=(1, 3), keepdims=True)
    row_scale = lax.rsqrt(square_sum / full_width + EPS)
    gain = norm_gain.astype(jnp.float32).reshape(1, loops, 1, width)
    normed = lax.optimization_barrier((values * row_scale * gain).astype(jnp.bfloat16))

    both_w = jnp.concatenate([w_gate, w_up], axis=1)
    both_w = both_w.reshape(2 * pairs_here * hidden_width, loops, width)
    down_w = w_down.reshape(pairs_here * hidden_width, loops, width)
    both = jnp.einsum("dljf,ulf->dju", normed, both_w, preferred_element_type=jnp.float32)
    gate, up = jnp.split(both, 2, axis=2)
    hidden = lax.optimization_barrier((jax.nn.silu(gate) * up).astype(jnp.bfloat16))
    part = jnp.einsum("dju,ulf->dljf", hidden, down_w, preferred_element_type=jnp.float32)
    part = part.astype(jnp.bfloat16)

    back = part.reshape(groups * loops * CAP, width)
    returned = lax.all_to_all(back, BOTH, 0, 0, tiled=True)
    returned = returned.reshape(groups, group_experts, hgroups, CAP, width).astype(jnp.float32)
    per_expert = jnp.sum(returned, axis=2).reshape(EXPERTS * CAP, width)

    weight_of = jnp.sum(jnp.where(chosen, route_weights[:, :, None], 0.0), axis=1)
    combine = jnp.where(pick3, weight_of[:, :, None], 0.0).reshape(rows, EXPERTS * CAP)
    mixed = jnp.dot(combine, per_expert, precision=lax.Precision.HIGHEST, preferred_element_type=jnp.float32)
    return (tokens.astype(jnp.float32) + mixed).astype(jnp.bfloat16)


def solution(mesh):
    return jax.shard_map(
        shards,
        mesh=mesh,
        in_specs=(
            P("dp", "loop"),
            P(),
            P("dp", None),
            P("dp", None),
            P(BOTH, None, None),
            P(BOTH, None, None),
            P(BOTH, None, None),
        ),
        out_specs=P("dp", "loop"),
        check_vma=False,
    )
```

```python
import jax
import jax.numpy as jnp
from jax import lax
from jax.sharding import PartitionSpec as P

EXPERTS = 128
HGROUPS = 4
CAP = 16
EPS = 1e-06
BOTH = ("dp", "loop")


def shards(tokens, norm_gain, route_ids, route_weights, w_gate, w_up, w_down):
    rows, width = tokens.shape
    top = route_ids.shape[1]
    groups = lax.axis_size("dp")
    loops = lax.axis_size("loop")
    pairs_here, hidden_width, full_width = w_gate.shape
    group_experts = EXPERTS // groups
    hgroups = loops // group_experts

    chosen = route_ids[:, :, None] == jnp.arange(EXPERTS, dtype=jnp.int32)[None, None, :]
    chose = jnp.any(chosen, axis=1)
    earlier = (jnp.arange(rows)[None, :] < jnp.arange(rows)[:, None]).astype(jnp.bfloat16)
    before = jnp.dot(earlier, chose.astype(jnp.bfloat16), preferred_element_type=jnp.float32)
    place = jnp.where(chose, before.astype(jnp.int32) + 1, 0)
    pick3 = place[:, :, None] == jnp.arange(1, CAP + 1, dtype=jnp.int32)[None, None, :]
    pick4 = jnp.broadcast_to(
        pick3.reshape(rows, groups, group_experts, 1, CAP),
        (rows, groups, group_experts, hgroups, CAP),
    ).reshape(rows, groups * loops * CAP).astype(jnp.bfloat16)
    send = jnp.dot(pick4.T, tokens, preferred_element_type=jnp.float32).astype(jnp.bfloat16)
    arrived = lax.all_to_all(send, BOTH, 0, 0, tiled=True)
    arrived = arrived.reshape(groups, loops, CAP, width)

    values = arrived.astype(jnp.float32)
    square_sum = jnp.sum(values * values, axis=(1, 3), keepdims=True)
    row_scale = lax.rsqrt(square_sum / full_width + EPS)
    gain = norm_gain.astype(jnp.float32).reshape(1, loops, 1, width)
    normed = lax.optimization_barrier((values * row_scale * gain).astype(jnp.bfloat16))

    both_w = jnp.concatenate([w_gate, w_up], axis=1)
    both_w = both_w.reshape(2 * pairs_here * hidden_width, loops, width)
    down_w = w_down.reshape(pairs_here * hidden_width, loops, width)
    both = jnp.einsum("dljf,ulf->dju", normed, both_w, preferred_element_type=jnp.float32)
    gate, up = jnp.split(both, 2, axis=2)
    hidden = lax.optimization_barrier((jax.nn.silu(gate) * up).astype(jnp.bfloat16))
    part = jnp.einsum("dju,ulf->dljf", hidden, down_w, preferred_element_type=jnp.float32)
    part = part.astype(jnp.bfloat16)

    back = part.reshape(groups * loops * CAP, width)
    returned = lax.all_to_all(back, BOTH, 0, 0, tiled=True)
    returned = returned.reshape(groups, group_experts, hgroups, CAP, width).astype(jnp.float32)
    per_expert = jnp.sum(returned, axis=2).reshape(EXPERTS * CAP, width)

    weight_of = jnp.sum(jnp.where(chosen, route_weights[:, :, None], 0.0), axis=1)
    combine = jnp.where(pick3, weight_of[:, :, None], 0.0).reshape(rows, EXPERTS * CAP)
    mixed = jnp.dot(combine, per_expert, precision=lax.Precision.HIGHEST, preferred_element_type=jnp.float32)
    return (tokens.astype(jnp.float32) + mixed).astype(jnp.bfloat16)


def solution(mesh):
    return jax.shard_map(
        shards,
        mesh=mesh,
        in_specs=(
            P("dp", "loop"),
            P(),
            P("dp", None),
            P("dp", None),
            P(BOTH, None, None),
            P(BOTH, None, None),
            P(BOTH, None, None),
        ),
        out_specs=P("dp", "loop"),
        check_vma=False,
    )
```

```python
import jax
import jax.numpy as jnp
from jax import lax
from jax.sharding import PartitionSpec as P

EXPERTS = 128
HGROUPS = 4
CAP = 16
EPS = 1e-06
BOTH = ("dp", "loop")


def shards(tokens, norm_gain, route_ids, route_weights, w_gate, w_up, w_down):
    rows, width = tokens.shape
    top = route_ids.shape[1]
    groups = lax.axis_size("dp")
    loops = lax.axis_size("loop")
    pairs_here, hidden_width, full_width = w_gate.shape
    group_experts = EXPERTS // groups
    hgroups = loops // group_experts

    chosen = route_ids[:, :, None] == jnp.arange(EXPERTS, dtype=jnp.int32)[None, None, :]
    chose = jnp.any(chosen, axis=1)
    earlier = (jnp.arange(rows)[None, :] < jnp.arange(rows)[:, None]).astype(jnp.bfloat16)
    before = jnp.dot(earlier, chose.astype(jnp.bfloat16), preferred_element_type=jnp.float32)
    place = jnp.where(chose, before.astype(jnp.int32) + 1, 0)
    pick3 = place[:, :, None] == jnp.arange(1, CAP + 1, dtype=jnp.int32)[None, None, :]
    pick = pick3.reshape(rows, EXPERTS * CAP).astype(jnp.bfloat16)
    gathered = jnp.dot(pick.T, tokens, preferred_element_type=jnp.float32).astype(jnp.bfloat16)
    gathered = gathered.reshape(groups, group_experts, 1, CAP, width)
    send = jnp.broadcast_to(gathered, (groups, group_experts, hgroups, CAP, width))
    send = send.reshape(groups * loops * CAP, width)
    arrived = lax.all_to_all(send, BOTH, 0, 0, tiled=True)
    arrived = arrived.reshape(groups, loops, CAP, width)

    values = arrived.astype(jnp.float32)
    square_sum = jnp.sum(values * values, axis=(1, 3), keepdims=True)
    row_scale = lax.rsqrt(square_sum / full_width + EPS)
    gain = norm_gain.astype(jnp.float32).reshape(1, loops, 1, width)
    normed = lax.optimization_barrier((values * row_scale * gain).astype(jnp.bfloat16))

    gate_w = w_gate.reshape(pairs_here * hidden_width, loops, width)
    up_w = w_up.reshape(pairs_here * hidden_width, loops, width)
    down_w = w_down.reshape(pairs_here * hidden_width, loops, width)
    gate = jnp.einsum("dljf,ulf->dju", normed, gate_w, preferred_element_type=jnp.float32)
    up = jnp.einsum("dljf,ulf->dju", normed, up_w, preferred_element_type=jnp.float32)
    hidden = lax.optimization_barrier((jax.nn.silu(gate) * up).astype(jnp.bfloat16))
    part = jnp.einsum("dju,ulf->dljf", hidden, down_w, preferred_element_type=jnp.float32)
    part = part.astype(jnp.bfloat16)

    back = part.reshape(groups * loops * CAP, width)
    returned = lax.all_to_all(back, BOTH, 0, 0, tiled=True)
    returned = returned.reshape(groups, group_experts, hgroups, CAP, width).astype(jnp.float32)
    per_expert = jnp.sum(returned, axis=2).reshape(EXPERTS * CAP, width)

    weight_of = jnp.sum(jnp.where(chosen, route_weights[:, :, None], 0.0), axis=1)
    combine = jnp.where(pick3, weight_of[:, :, None], 0.0).reshape(rows, EXPERTS * CAP)
    mixed = jnp.dot(combine, per_expert, precision=lax.Precision.HIGH, preferred_element_type=jnp.float32)
    return (tokens.astype(jnp.float32) + mixed).astype(jnp.bfloat16)


def solution(mesh):
    return jax.shard_map(
        shards,
        mesh=mesh,
        in_specs=(
            P("dp", "loop"),
            P(),
            P("dp", None),
            P("dp", None),
            P(BOTH, None, None),
            P(BOTH, None, None),
            P(BOTH, None, None),
        ),
        out_specs=P("dp", "loop"),
        check_vma=False,
    )
```

```python
import jax
import jax.numpy as jnp
from jax import lax
from jax.experimental import pallas as pl
from jax.experimental.pallas import tpu as pltpu
from jax.sharding import PartitionSpec as P

EXPERTS = 128
HGROUPS = 4
CAP = 16
EPS = 1e-06
BOTH = ("dp", "loop")


def expert_body(x_ref, g_ref, wg_ref, wu_ref, wd_ref, o_ref, normed_ref, acc_ref):
    step = pl.program_id(0)
    blocks, loops, slots, width = x_ref.shape
    rows = blocks * slots

    @pl.when(step == 0)
    def _():
        total = jnp.zeros((rows, 1), jnp.float32)
        for l in range(loops):
            v = x_ref[:, l, :, :].reshape(rows, width).astype(jnp.float32)
            total = total + jnp.sum(v * v, axis=1, keepdims=True)
        scale = lax.rsqrt(total / (loops * width) + EPS)
        for l in range(loops):
            v = x_ref[:, l, :, :].reshape(rows, width).astype(jnp.float32)
            normed_ref[:, l * width:(l + 1) * width] = (v * scale * g_ref[l:l + 1, :]).astype(jnp.bfloat16)
        acc_ref[...] = jnp.zeros_like(acc_ref)

    normed = normed_ref[...]
    nt = (((1,), (1,)), ((), ()))
    gate = lax.dot_general(normed, wg_ref[...], nt, preferred_element_type=jnp.float32)
    up = lax.dot_general(normed, wu_ref[...], nt, preferred_element_type=jnp.float32)
    hidden = (gate / (1.0 + jnp.exp(-gate)) * up).astype(jnp.bfloat16)
    acc_ref[...] += jnp.dot(hidden, wd_ref[...], preferred_element_type=jnp.float32)

    @pl.when(step == pl.num_programs(0) - 1)
    def _():
        for l in range(loops):
            o_ref[:, l, :, :] = acc_ref[:, l * width:(l + 1) * width].astype(jnp.bfloat16).reshape(blocks, slots, width)


def expert_ffn(arrived, gain, wg, wu, wd, chunk=128):
    blocks, loops, slots, width = arrived.shape
    hidden_width, full = wg.shape
    rows = blocks * slots
    steps = hidden_width // chunk
    whole = lambda i: (0, 0, 0, 0)
    return pl.pallas_call(
        expert_body,
        grid=(steps,),
        in_specs=[
            pl.BlockSpec((blocks, loops, slots, width), whole),
            pl.BlockSpec((loops, width), lambda i: (0, 0)),
            pl.BlockSpec((chunk, full), lambda i: (i, 0)),
            pl.BlockSpec((chunk, full), lambda i: (i, 0)),
            pl.BlockSpec((chunk, full), lambda i: (i, 0)),
        ],
        out_specs=pl.BlockSpec((blocks, loops, slots, width), whole),
        out_shape=jax.ShapeDtypeStruct(arrived.shape, jnp.bfloat16),
        scratch_shapes=[pltpu.VMEM((rows, full), jnp.bfloat16), pltpu.VMEM((rows, full), jnp.float32)],
        compiler_params=pltpu.CompilerParams(dimension_semantics=("arbitrary",)),
        cost_estimate=pl.CostEstimate(
            flops=6 * rows * hidden_width * full,
            transcendentals=rows * hidden_width,
            bytes_accessed=2 * arrived.size * 2 + 3 * hidden_width * full * 2,
        ),
    )(arrived, gain, wg, wu, wd)


def shards(tokens, norm_gain, route_ids, route_weights, w_gate, w_up, w_down):
    rows, width = tokens.shape
    top = route_ids.shape[1]
    groups = lax.axis_size("dp")
    loops = lax.axis_size("loop")
    pairs_here, hidden_width, full_width = w_gate.shape
    group_experts = EXPERTS // groups
    hgroups = loops // group_experts

    chosen = route_ids[:, :, None] == jnp.arange(EXPERTS, dtype=jnp.int32)[None, None, :]
    chose = jnp.any(chosen, axis=1)
    earlier = (jnp.arange(rows)[None, :] < jnp.arange(rows)[:, None]).astype(jnp.bfloat16)
    before = jnp.dot(earlier, chose.astype(jnp.bfloat16), preferred_element_type=jnp.float32)
    place = jnp.where(chose, before.astype(jnp.int32) + 1, 0)
    pick3 = place[:, :, None] == jnp.arange(1, CAP + 1, dtype=jnp.int32)[None, None, :]
    pick = pick3.reshape(rows, EXPERTS * CAP).astype(jnp.bfloat16)
    gathered = jnp.dot(pick.T, tokens, preferred_element_type=jnp.float32).astype(jnp.bfloat16)
    gathered = gathered.reshape(groups, group_experts, 1, CAP, width)
    send = jnp.broadcast_to(gathered, (groups, group_experts, hgroups, CAP, width))
    send = send.reshape(groups * loops * CAP, width)
    arrived = lax.all_to_all(send, BOTH, 0, 0, tiled=True)
    arrived = arrived.reshape(groups, loops, CAP, width)

    gain = norm_gain.astype(jnp.float32).reshape(loops, width)
    part = expert_ffn(
        arrived,
        gain,
        w_gate.reshape(pairs_here * hidden_width, full_width),
        w_up.reshape(pairs_here * hidden_width, full_width),
        w_down.reshape(pairs_here * hidden_width, full_width),
    )

    back = part.reshape(groups * loops * CAP, width)
    returned = lax.all_to_all(back, BOTH, 0, 0, tiled=True)
    returned = returned.reshape(groups, group_experts, hgroups, CAP, width).astype(jnp.float32)
    per_expert = jnp.sum(returned, axis=2).reshape(EXPERTS * CAP, width)

    weight_of = jnp.sum(jnp.where(chosen, route_weights[:, :, None], 0.0), axis=1)
    combine = jnp.where(pick3, weight_of[:, :, None], 0.0).reshape(rows, EXPERTS * CAP)
    mixed = jnp.dot(combine, per_expert, precision=lax.Precision.HIGH, preferred_element_type=jnp.float32)
    return (tokens.astype(jnp.float32) + mixed).astype(jnp.bfloat16)


def solution(mesh):
    return jax.shard_map(
        shards,
        mesh=mesh,
        in_specs=(
            P("dp", "loop"),
            P(),
            P("dp", None),
            P("dp", None),
            P(BOTH, None, None),
            P(BOTH, None, None),
            P(BOTH, None, None),
        ),
        out_specs=P("dp", "loop"),
        check_vma=False,
    )
```

```python
import jax
import jax.numpy as jnp
from jax import lax
from jax.sharding import PartitionSpec as P

EXPERTS = 128
HGROUPS = 4
CAP = 16
EPS = 1e-06
BOTH = ("dp", "loop")


def shards(tokens, norm_gain, route_ids, route_weights, w_gate, w_up, w_down):
    rows, width = tokens.shape
    top = route_ids.shape[1]
    groups = lax.axis_size("dp")
    loops = lax.axis_size("loop")
    pairs_here, hidden_width, full_width = w_gate.shape
    group_experts = EXPERTS // groups
    hgroups = loops // group_experts

    chosen = route_ids.T[:, :, None] == jnp.arange(EXPERTS, dtype=jnp.int32)[None, None, :]
    chose = jnp.any(chosen, axis=0)
    earlier = (jnp.arange(rows)[None, :] < jnp.arange(rows)[:, None]).astype(jnp.bfloat16)
    before = jnp.dot(earlier, chose.astype(jnp.bfloat16), preferred_element_type=jnp.float32)
    place = jnp.where(chose, before.astype(jnp.int32) + 1, 0)
    pick3 = place[:, :, None] == jnp.arange(1, CAP + 1, dtype=jnp.int32)[None, None, :]
    pick = pick3.reshape(rows, EXPERTS * CAP).astype(jnp.bfloat16)
    gathered = jnp.dot(pick.T, tokens, preferred_element_type=jnp.float32).astype(jnp.bfloat16)
    gathered = gathered.reshape(groups, group_experts, 1, CAP, width)
    send = jnp.broadcast_to(gathered, (groups, group_experts, hgroups, CAP, width))
    send = send.reshape(groups * loops * CAP, width)
    arrived = lax.all_to_all(send, BOTH, 0, 0, tiled=True)
    arrived = arrived.reshape(groups, loops, CAP, width)

    values = arrived.astype(jnp.float32)
    square_sum = jnp.sum(values * values, axis=(1, 3), keepdims=True)
    row_scale = lax.rsqrt(square_sum / full_width + EPS)
    gain = norm_gain.astype(jnp.float32).reshape(1, loops, 1, width)
    normed = lax.optimization_barrier((values * row_scale * gain).astype(jnp.bfloat16))

    gate_w = w_gate.reshape(pairs_here * hidden_width, loops, width)
    up_w = w_up.reshape(pairs_here * hidden_width, loops, width)
    down_w = w_down.reshape(pairs_here * hidden_width, loops, width)
    gate = jnp.einsum("dljf,ulf->dju", normed, gate_w, preferred_element_type=jnp.float32)
    up = jnp.einsum("dljf,ulf->dju", normed, up_w, preferred_element_type=jnp.float32)
    hidden = lax.optimization_barrier((jax.nn.silu(gate) * up).astype(jnp.bfloat16))
    part = jnp.einsum("dju,ulf->dljf", hidden, down_w, preferred_element_type=jnp.float32)
    part = part.astype(jnp.bfloat16)

    back = part.reshape(groups * loops * CAP, width)
    returned = lax.all_to_all(back, BOTH, 0, 0, tiled=True)
    returned = returned.reshape(groups, group_experts, hgroups, CAP, width).astype(jnp.float32)
    per_expert = jnp.sum(returned, axis=2).reshape(EXPERTS * CAP, width)

    weight_of = jnp.sum(jnp.where(chosen, route_weights.T[:, :, None], 0.0), axis=0)
    combine = jnp.where(pick3, weight_of[:, :, None], 0.0).reshape(rows, EXPERTS * CAP)
    mixed = jnp.dot(combine, per_expert, precision=lax.Precision.HIGH, preferred_element_type=jnp.float32)
    return (tokens.astype(jnp.float32) + mixed).astype(jnp.bfloat16)


def solution(mesh):
    return jax.shard_map(
        shards,
        mesh=mesh,
        in_specs=(
            P("dp", "loop"),
            P(),
            P("dp", None),
            P("dp", None),
            P(BOTH, None, None),
            P(BOTH, None, None),
            P(BOTH, None, None),
        ),
        out_specs=P("dp", "loop"),
        check_vma=False,
    )
```

```python
import jax
import jax.numpy as jnp
from jax import lax
from jax.sharding import PartitionSpec as P

EXPERTS = 128
HGROUPS = 4
CAP = 16
EPS = 1e-06
BOTH = ("dp", "loop")


def shards(tokens, norm_gain, route_ids, route_weights, w_gate, w_up, w_down):
    rows, width = tokens.shape
    top = route_ids.shape[1]
    groups = lax.axis_size("dp")
    loops = lax.axis_size("loop")
    pairs_here, hidden_width, full_width = w_gate.shape
    group_experts = EXPERTS // groups
    hgroups = loops // group_experts

    chosen = route_ids[:, :, None] == jnp.arange(EXPERTS, dtype=jnp.int32)[None, None, :]
    chose = jnp.any(chosen, axis=1)
    earlier = (jnp.arange(rows)[None, :] < jnp.arange(rows)[:, None]).astype(jnp.bfloat16)
    before = jnp.dot(earlier, chose.astype(jnp.bfloat16), preferred_element_type=jnp.float32)
    place = jnp.where(chose, before.astype(jnp.int32) + 1, 0)
    pick3 = place[:, :, None] == jnp.arange(1, CAP + 1, dtype=jnp.int32)[None, None, :]
    pick = pick3.reshape(rows, EXPERTS * CAP).astype(jnp.bfloat16)
    gathered = jnp.dot(pick.T, tokens, preferred_element_type=jnp.float32).astype(jnp.bfloat16)
    gathered = gathered.reshape(groups, group_experts, 1, CAP, width)
    send = jnp.broadcast_to(gathered, (groups, group_experts, hgroups, CAP, width))
    send = send.reshape(groups * loops * CAP, width)
    arrived = lax.all_to_all(send, BOTH, 0, 0, tiled=True)
    arrived = arrived.reshape(groups, loops, CAP, width)

    values = arrived.astype(jnp.float32)
    across = lax.optimization_barrier(jnp.sum(values * values, axis=1))
    square_sum = jnp.sum(across, axis=2)[:, None, :, None]
    row_scale = lax.rsqrt(square_sum / full_width + EPS)
    gain = norm_gain.astype(jnp.float32).reshape(1, loops, 1, width)
    normed = lax.optimization_barrier((values * row_scale * gain).astype(jnp.bfloat16))

    gate_w = w_gate.reshape(pairs_here * hidden_width, loops, width)
    up_w = w_up.reshape(pairs_here * hidden_width, loops, width)
    down_w = w_down.reshape(pairs_here * hidden_width, loops, width)
    gate = jnp.einsum("dljf,ulf->dju", normed, gate_w, preferred_element_type=jnp.float32)
    up = jnp.einsum("dljf,ulf->dju", normed, up_w, preferred_element_type=jnp.float32)
    hidden = lax.optimization_barrier((jax.nn.silu(gate) * up).astype(jnp.bfloat16))
    part = jnp.einsum("dju,ulf->dljf", hidden, down_w, preferred_element_type=jnp.float32)
    part = part.astype(jnp.bfloat16)

    back = part.reshape(groups * loops * CAP, width)
    returned = lax.all_to_all(back, BOTH, 0, 0, tiled=True)
    returned = returned.reshape(groups, group_experts, hgroups, CAP, width).astype(jnp.float32)
    per_expert = jnp.sum(returned, axis=2).reshape(EXPERTS * CAP, width)

    weight_of = jnp.sum(jnp.where(chosen, route_weights[:, :, None], 0.0), axis=1)
    combine = jnp.where(pick3, weight_of[:, :, None], 0.0).reshape(rows, EXPERTS * CAP)
    mixed = jnp.dot(combine, per_expert, precision=lax.Precision.HIGH, preferred_element_type=jnp.float32)
    return (tokens.astype(jnp.float32) + mixed).astype(jnp.bfloat16)


def solution(mesh):
    return jax.shard_map(
        shards,
        mesh=mesh,
        in_specs=(
            P("dp", "loop"),
            P(),
            P("dp", None),
            P("dp", None),
            P(BOTH, None, None),
            P(BOTH, None, None),
            P(BOTH, None, None),
        ),
        out_specs=P("dp", "loop"),
        check_vma=False,
    )
```

```python
import jax
import jax.numpy as jnp
from jax import lax
from jax.sharding import PartitionSpec as P

EXPERTS = 128
HGROUPS = 4
CAP = 16
EPS = 1e-06
BOTH = ("dp", "loop")


def shards(tokens, norm_gain, route_ids, route_weights, w_gate, w_up, w_down):
    rows, width = tokens.shape
    top = route_ids.shape[1]
    groups = lax.axis_size("dp")
    loops = lax.axis_size("loop")
    pairs_here, hidden_width, full_width = w_gate.shape
    group_experts = EXPERTS // groups
    hgroups = loops // group_experts

    chosen = route_ids.T[:, :, None] == jnp.arange(EXPERTS, dtype=jnp.int32)[None, None, :]
    chose = jnp.any(chosen, axis=0)
    earlier = (jnp.arange(rows)[None, :] < jnp.arange(rows)[:, None]).astype(jnp.bfloat16)
    before = jnp.dot(earlier, chose.astype(jnp.bfloat16), preferred_element_type=jnp.float32)
    place = jnp.where(chose, before.astype(jnp.int32) + 1, 0)
    pick3 = place[:, :, None] == jnp.arange(1, CAP + 1, dtype=jnp.int32)[None, None, :]
    pick = pick3.reshape(rows, EXPERTS * CAP).astype(jnp.bfloat16)
    gathered = jnp.dot(pick.T, tokens, preferred_element_type=jnp.float32).astype(jnp.bfloat16)
    gathered = gathered.reshape(groups, group_experts, 1, CAP, width)
    send = jnp.broadcast_to(gathered, (groups, group_experts, hgroups, CAP, width))
    send = send.reshape(groups * loops * CAP, width)
    arrived = lax.all_to_all(send, BOTH, 0, 0, tiled=True)
    arrived = arrived.reshape(groups, loops, CAP, width)

    values = arrived.astype(jnp.float32)
    across = lax.optimization_barrier(jnp.sum(values * values, axis=1))
    square_sum = jnp.sum(across, axis=2)[:, None, :, None]
    row_scale = lax.rsqrt(square_sum / full_width + EPS)
    gain = norm_gain.astype(jnp.float32).reshape(1, loops, 1, width)
    normed = lax.optimization_barrier((values * row_scale * gain).astype(jnp.bfloat16))

    gate_w = w_gate.reshape(pairs_here * hidden_width, loops, width)
    up_w = w_up.reshape(pairs_here * hidden_width, loops, width)
    down_w = w_down.reshape(pairs_here * hidden_width, loops, width)
    gate = jnp.einsum("dljf,ulf->dju", normed, gate_w, preferred_element_type=jnp.float32)
    up = jnp.einsum("dljf,ulf->dju", normed, up_w, preferred_element_type=jnp.float32)
    hidden = lax.optimization_barrier((jax.nn.silu(gate) * up).astype(jnp.bfloat16))
    part = jnp.einsum("dju,ulf->dljf", hidden, down_w, preferred_element_type=jnp.float32)
    part = part.astype(jnp.bfloat16)

    back = part.reshape(groups * loops * CAP, width)
    returned = lax.all_to_all(back, BOTH, 0, 0, tiled=True)
    returned = returned.reshape(groups, group_experts, hgroups, CAP, width).astype(jnp.float32)
    per_expert = jnp.sum(returned, axis=2).reshape(EXPERTS * CAP, width)

    weight_of = jnp.sum(jnp.where(chosen, route_weights.T[:, :, None], 0.0), axis=0)
    combine = jnp.where(pick3, weight_of[:, :, None], 0.0).reshape(rows, EXPERTS * CAP)
    mixed = jnp.dot(combine, per_expert, precision=lax.Precision.HIGH, preferred_element_type=jnp.float32)
    return (tokens.astype(jnp.float32) + mixed).astype(jnp.bfloat16)


def solution(mesh):
    return jax.shard_map(
        shards,
        mesh=mesh,
        in_specs=(
            P("dp", "loop"),
            P(),
            P("dp", None),
            P("dp", None),
            P(BOTH, None, None),
            P(BOTH, None, None),
            P(BOTH, None, None),
        ),
        out_specs=P("dp", "loop"),
        check_vma=False,
    )
```
